32 devices in a mesh: groups: 2 (over y), dp: 4 (over z), tensor: 2 (over x), layer: 2 (over core).
Axes of the slice: x: 2, y: 2, z: 4, core: 2. Of those that a mesh axis runs over, the one named last changes fastest.
Arguments:
- hidden_in: bfloat16 [2, 8, 512, 14336], P('layer', ('groups', 'dp'), None, 'tensor'), parts along dimension 1, may hold values from -6 to 6
- out_grad: bfloat16 [2, 8, 512, 4096], P('layer', ('groups', 'dp'), 'tensor'), parts along dimension 1, may hold values from -6 to 6
- proj_in: bfloat16 [2, 14336, 64], P('layer', 'tensor'), may hold values from -0.046875 to 0.046875
- proj_out: bfloat16 [2, 4096, 64], P('layer'), may hold values from -0.09375 to 0.09375
- query_grads: bfloat16 [2, 1024, 4096], P('layer', 'dp', 'tensor'), may hold values from -1.5 to 1.5
- lengths: int32 [8], P(('groups', 'dp')), parts along dimension 0, may hold values from 128 to 512, as said below
- query_decision: int32 [1024], P('dp'), may hold values from 0 to 1023
Outputs:
- influence: float32 [8, 1024], P(('groups', 'dp')), parts along dimension 0
The draws below stay inside these ranges and needn't reach their ends.
There are 2 independent parts, one for each index of `groups`. The reference program is written for one: setup_inputs(seed, part) draws one part's arguments, and reference() takes and returns one part's arrays. A program takes and returns all parts, laid end to end along the dimension named above; an argument that names none is the same for every part. Nothing has to cross between parts.
Inputs may be any that keep to these rules, and one draw needn't show every extreme that they name: `lengths`: in each part one transcript has all 512 tokens live and another has exactly 128.
All inputs are finite; a program needn't handle non-finite values.
Results may differ from the reference program's by a relative error of at most 0.004.
Values may be sent and summed in bfloat16 or wider, within the bound.
No kernel may reach another device: no remote copies, remote signals or barrier semaphores. Data moves between devices by JAX's collectives and lax.ppermute only.
A program may use at most 64 MiB of HBM per device.

```python
import jax
import jax.numpy as jnp
from jax import lax

D = 4096
FF = 14336
PROJ = 64
LEN = 512
DECISIONS = 1024
LAYERS = 2
EXAMPLES = 4
QUERIES = 1024


def draw_lengths(key, part):
    base = jax.random.randint(jax.random.fold_in(key, 11), (EXAMPLES,), LEN // 4, LEN + 1)
    chosen = jax.random.randint(jax.random.fold_in(key, 12), (), 0, EXAMPLES)
    shorter = (chosen + 1) % EXAMPLES
    slots = jnp.arange(EXAMPLES)
    base = jnp.where(slots == shorter, LEN // 4, base)
    return jnp.where(slots == chosen, LEN, base).astype(jnp.int32)


def with_ends(result, rng, smallest, largest):
    longest = result.shape.index(max(result.shape))
    spots = []
    for shift in (0, 1):
        where = [jax.random.randint(jax.random.fold_in(rng, axis), (), 0, length) for axis, length in enumerate(result.shape)]
        where[longest] = (where[longest] + shift) % result.shape[longest]
        spots.append(tuple(where))
    return result.at[spots[0]].set(smallest).at[spots[1]].set(largest)


def block_levels(own_key, shape, split, low, largest):
    level = 1.0
    for position, blocks in split:
        heights = jax.random.uniform(jax.random.fold_in(jax.random.fold_in(own_key, 6), position), (blocks,), jnp.float32, low / len(split), largest / len(split))
        level = level * jnp.repeat(jnp.exp(heights), shape[position] // blocks).reshape((-1,) + (1,) * (len(shape) - 1 - position))
    return level


def bell_draw(key, extent, width, most, split=(), kind=jnp.bfloat16):
    drawn = width * jax.random.normal(key, extent, jnp.float32)
    if split:
        drawn = drawn * block_levels(key, extent, split, -0.22, 0.18)
    return jnp.clip(drawn, -most, most).astype(kind)


def setup_inputs(seed: int = 0, part: int = 0) -> dict:
    keys = jax.random.split(jax.random.key(seed), 8)
    part_keys = jax.random.split(jax.random.fold_in(keys[7], part), 8)
    return {
        "hidden_in": bell_draw(part_keys[0], (LAYERS, EXAMPLES, LEN, FF), 1.0, 6.0, ((0, 2), (1, 4), (3, 2))),
        "out_grad": bell_draw(part_keys[1], (LAYERS, EXAMPLES, LEN, D), 1.0, 6.0, ((0, 2), (1, 4), (2, 2))),
        "proj_in": bell_draw(keys[2], (LAYERS, FF, PROJ), FF ** -0.5, 0.046875, ((0, 2), (1, 2))),
        "proj_out": bell_draw(keys[3], (LAYERS, D, PROJ), D ** -0.5, 0.09375, ((0, 2),)),
        "query_grads": bell_draw(keys[4], (LAYERS, QUERIES, PROJ * PROJ), 0.25, 1.5, ((0, 2), (1, 4), (2, 2))),
        "lengths": draw_lengths(jax.random.fold_in(jax.random.fold_in(keys[7], part), 71), part),
        "query_decision": with_ends(jax.random.randint(keys[6], (QUERIES,), 0, DECISIONS), jax.random.fold_in(keys[6], 1), 0, DECISIONS - 1).astype(jnp.int32),
    }


def layer_scores(hidden_in, out_grad, proj_in, proj_out, query_grads, lengths, layer):
    positions = jnp.arange(LEN, dtype=jnp.int32)
    side_hidden = proj_in[layer].astype(jnp.float32)
    side_width = proj_out[layer].astype(jnp.float32)

    def one_example(index):
        hidden_rows = hidden_in[layer, index].astype(jnp.float32)
        grad_rows = out_grad[layer, index].astype(jnp.float32)
        left = jnp.dot(hidden_rows, side_hidden, precision=lax.Precision.HIGHEST)
        right = jnp.dot(grad_rows, side_width, precision=lax.Precision.HIGHEST)
        live_tokens = (positions < lengths[index]).astype(jnp.float32)
        right = (right * live_tokens[:, None]).astype(jnp.bfloat16)
        block = jnp.dot(left.T, right.astype(jnp.float32), precision=lax.Precision.HIGHEST)
        block = block / lengths[index].astype(jnp.float32)
        return block.astype(jnp.bfloat16).reshape(PROJ * PROJ)

    blocks = lax.map(one_example, jnp.arange(EXAMPLES, dtype=jnp.int32))
    return jnp.dot(blocks.astype(jnp.float32), query_grads[layer].astype(jnp.float32).T, precision=lax.Precision.HIGHEST)


def reference(hidden_in, out_grad, proj_in, proj_out, query_grads, lengths, query_decision):
    scores = layer_scores(hidden_in, out_grad, proj_in, proj_out, query_grads, lengths, 0)
    scores = scores + layer_scores(hidden_in, out_grad, proj_in, proj_out, query_grads, lengths, 1)
    onehot = (query_decision[:, None] == jnp.arange(DECISIONS, dtype=jnp.int32)[None, :]).astype(jnp.float32)
    return jnp.dot(scores, onehot, precision=lax.Precision.HIGHEST)
```

```python
import jax
import jax.numpy as jnp
from jax import lax
from jax.sharding import PartitionSpec as P

DECISIONS = 1024


def body(hidden_in, out_grad, proj_in, proj_out, query_grads, lengths, query_decision):
    hidden_rows = hidden_in[0, 0]
    grad_rows = out_grad[0, 0]
    side_hidden = proj_in[0]
    side_width = proj_out[0]
    query_rows = query_grads[0]
    length = lengths[0]
    seq_shard = grad_rows.shape[0]
    first_pos = lax.axis_index("tensor") * seq_shard
    positions = first_pos + jnp.arange(seq_shard, dtype=jnp.int32)
    live = (positions < length).astype(jnp.float32)
    right = jnp.dot(grad_rows, side_width, preferred_element_type=jnp.float32)
    right = (right * live[:, None]).astype(jnp.bfloat16)
    right_full = lax.all_gather(right, "tensor", axis=0, tiled=True)
    left = jnp.dot(hidden_rows, side_hidden, preferred_element_type=jnp.float32)
    partial = jnp.dot(
        left.T, right_full.astype(jnp.float32), precision=lax.Precision.HIGHEST
    )
    partial = partial / length.astype(jnp.float32)
    grad_part = lax.psum_scatter(partial, "tensor", scatter_dimension=0, tiled=True)
    grad_flat = grad_part.reshape(1, -1).astype(jnp.bfloat16)
    grads_all = lax.all_gather(grad_flat, "dp", axis=0, tiled=True)
    scores = jnp.dot(grads_all, query_rows.T, preferred_element_type=jnp.float32)
    table = (
        query_decision[:, None] == jnp.arange(DECISIONS, dtype=jnp.int32)[None, :]
    ).astype(jnp.float32)
    partial_dec = jnp.dot(scores, table, precision=lax.Precision.HIGHEST)
    total = lax.psum(partial_dec, ("dp", "tensor", "layer"))
    row = lax.dynamic_slice_in_dim(total, lax.axis_index("dp"), 1, axis=0)
    return row


def solution(mesh):
    in_specs = (
        P("layer", ("groups", "dp"), None, "tensor"),
        P("layer", ("groups", "dp"), "tensor", None),
        P("layer", "tensor", None),
        P("layer", None, None),
        P("layer", "dp", "tensor"),
        P(("groups", "dp")),
        P("dp"),
    )
    out_specs = P(("groups", "dp"), None)
    return jax.shard_map(body, mesh=mesh, in_specs=in_specs, out_specs=out_specs, check_vma=False)
```

```python
import jax
import jax.numpy as jnp
from jax import lax
from jax.sharding import PartitionSpec as P

DECISIONS = 1024


def shifted(x, axis, size, shift):
    return lax.ppermute(x, axis, [(i, (i + shift) % size) for i in range(size)])


def body(hidden_in, out_grad, proj_in, proj_out, query_grads, lengths, query_decision):
    tensors = lax.axis_size("tensor")
    dps = lax.axis_size("dp")
    layers = lax.axis_size("layer")
    me_t = lax.axis_index("tensor")
    me_d = lax.axis_index("dp")
    hidden_rows = hidden_in[0, 0]
    grad_rows = out_grad[0, 0]
    query_rows = query_grads[0]
    length = lengths[0]
    seq_shard = grad_rows.shape[0]

    positions = me_t * seq_shard + jnp.arange(seq_shard, dtype=jnp.int32)
    live = (positions < length).astype(jnp.float32)
    right = jnp.dot(grad_rows, proj_out[0], preferred_element_type=jnp.float32)
    right = (right * live[:, None]).astype(jnp.bfloat16)
    received = [right] + [shifted(right, "tensor", tensors, s) for s in range(1, tensors)]

    left = jnp.dot(hidden_rows, proj_in[0], preferred_element_type=jnp.float32)
    partial = None
    for s, part in enumerate(received):
        owner = (me_t - s) % tensors
        rows = lax.dynamic_slice_in_dim(left, owner * seq_shard, seq_shard, axis=0)
        term = jnp.dot(rows.T, part.astype(jnp.float32), precision=lax.Precision.HIGHEST)
        partial = term if partial is None else partial + term

    block_rows = partial.shape[0] // tensors
    grad_part = lax.dynamic_slice_in_dim(partial, me_t * block_rows, block_rows, axis=0)
    for s in range(1, tensors):
        dest = (me_t + s) % tensors
        piece = lax.dynamic_slice_in_dim(partial, dest * block_rows, block_rows, axis=0)
        grad_part = grad_part + shifted(piece, "tensor", tensors, s)
    grad_part = grad_part / length.astype(jnp.float32)
    grad_flat = grad_part.reshape(1, -1).astype(jnp.bfloat16)

    grads = [grad_flat] + [shifted(grad_flat, "dp", dps, s) for s in range(1, dps)]
    grads = jnp.concatenate(grads, axis=0)
    scores = jnp.dot(grads, query_rows.T, preferred_element_type=jnp.float32)
    table = (
        query_decision[:, None] == jnp.arange(DECISIONS, dtype=jnp.int32)[None, :]
    ).astype(jnp.float32)
    partial_dec = jnp.dot(scores, table, precision=lax.Precision.HIGHEST)

    total = partial_dec[0:1]
    for s in range(1, dps):
        total = total + shifted(partial_dec[s : s + 1], "dp", dps, -s)
    if tensors > 1:
        if tensors == 2:
            total = total + shifted(total, "tensor", tensors, 1)
        else:
            total = lax.psum(total, "tensor")
    if layers == 2:
        total = total + shifted(total, "layer", layers, 1)
    else:
        total = lax.psum(total, "layer")
    return total


def solution(mesh):
    in_specs = (
        P("layer", ("groups", "dp"), None, "tensor"),
        P("layer", ("groups", "dp"), "tensor", None),
        P("layer", "tensor", None),
        P("layer", None, None),
        P("layer", "dp", "tensor"),
        P(("groups", "dp")),
        P("dp"),
    )
    out_specs = P(("groups", "dp"), None)
    return jax.shard_map(body, mesh=mesh, in_specs=in_specs, out_specs=out_specs, check_vma=False)
```

```python
import jax
import jax.numpy as jnp
from jax import lax
from jax.sharding import PartitionSpec as P

DECISIONS = 1024


def shifted(x, axis, size, shift):
    return lax.ppermute(x, axis, [(i, (i + shift) % size) for i in range(size)])


def body(hidden_in, out_grad, proj_in, proj_out, query_grads, lengths, query_decision):
    tensors = lax.axis_size("tensor")
    dps = lax.axis_size("dp")
    layers = lax.axis_size("layer")
    me_t = lax.axis_index("tensor")
    me_d = lax.axis_index("dp")
    hidden_rows = hidden_in[0, 0]
    grad_rows = out_grad[0, 0]
    query_own = query_grads[0]
    query_parts = [query_own] + [shifted(query_own, "tensor", tensors, s) for s in range(1, tensors)]
    length = lengths[0]
    seq_shard = grad_rows.shape[0]

    positions = me_t * seq_shard + jnp.arange(seq_shard, dtype=jnp.int32)
    live = (positions < length).astype(jnp.float32)
    right = jnp.dot(grad_rows, proj_out[0], preferred_element_type=jnp.float32)
    right = (right * live[:, None]).astype(jnp.bfloat16)
    received = [right] + [shifted(right, "tensor", tensors, s) for s in range(1, tensors)]

    left = jnp.dot(hidden_rows, proj_in[0], preferred_element_type=jnp.float32)
    partial = None
    for s, part in enumerate(received):
        owner = (me_t - s) % tensors
        rows = lax.dynamic_slice_in_dim(left, owner * seq_shard, seq_shard, axis=0)
        term = jnp.dot(rows.T, part.astype(jnp.float32), precision=lax.Precision.HIGHEST)
        partial = term if partial is None else partial + term

    total_grad = partial
    for s in range(1, tensors):
        total_grad = total_grad + shifted(partial, "tensor", tensors, s)
    total_grad = total_grad / length.astype(jnp.float32)
    grad_flat = total_grad.reshape(1, -1).astype(jnp.bfloat16)

    grads = [grad_flat] + [shifted(grad_flat, "dp", dps, s) for s in range(1, dps)]
    grads = jnp.concatenate(grads, axis=0)
    entry_block = query_own.shape[1]
    scores = None
    for s, part in enumerate(query_parts):
        owner = (me_t - s) % tensors
        cols = lax.dynamic_slice_in_dim(grads, owner * entry_block, entry_block, axis=1)
        term = jnp.dot(cols, part.T, preferred_element_type=jnp.float32)
        scores = term if scores is None else scores + term
    table = (
        query_decision[:, None] == jnp.arange(DECISIONS, dtype=jnp.int32)[None, :]
    ).astype(jnp.float32)
    partial_dec = jnp.dot(scores, table, precision=lax.Precision.HIGHEST)

    total = partial_dec[0:1]
    for s in range(1, dps):
        total = total + shifted(partial_dec[s : s + 1], "dp", dps, -s)
    if layers == 2:
        total = total + shifted(total, "layer", layers, 1)
    else:
        total = lax.psum(total, "layer")
    return total


def solution(mesh):
    in_specs = (
        P("layer", ("groups", "dp"), None, "tensor"),
        P("layer", ("groups", "dp"), "tensor", None),
        P("layer", "tensor", None),
        P("layer", None, None),
        P("layer", "dp", "tensor"),
        P(("groups", "dp")),
        P("dp"),
    )
    out_specs = P(("groups", "dp"), None)
    return jax.shard_map(body, mesh=mesh, in_specs=in_specs, out_specs=out_specs, check_vma=False)
```

```python
import jax
import jax.numpy as jnp
from jax import lax
from jax.sharding import PartitionSpec as P

DECISIONS = 1024


def shifted(x, axis, size, shift):
    return lax.ppermute(x, axis, [(i, (i + shift) % size) for i in range(size)])


def body(hidden_in, out_grad, proj_in, proj_out, query_grads, lengths, query_decision):
    tensors = lax.axis_size("tensor")
    dps = lax.axis_size("dp")
    layers = lax.axis_size("layer")
    me_t = lax.axis_index("tensor")
    hidden_rows = hidden_in[0, 0]
    grad_rows = out_grad[0, 0]
    query_rows = query_grads[0]
    length = lengths[0]
    seq_shard = grad_rows.shape[0]

    positions = me_t * seq_shard + jnp.arange(seq_shard, dtype=jnp.int32)
    live = (positions < length).astype(jnp.float32)
    right = jnp.dot(grad_rows, proj_out[0], preferred_element_type=jnp.float32)
    right = (right * live[:, None]).astype(jnp.bfloat16)
    received = [right] + [shifted(right, "tensor", tensors, s) for s in range(1, tensors)]

    left = jnp.dot(hidden_rows, proj_in[0], preferred_element_type=jnp.float32)
    partial = None
    for s, part in enumerate(received):
        owner = (me_t - s) % tensors
        rows = lax.dynamic_slice_in_dim(left, owner * seq_shard, seq_shard, axis=0)
        term = jnp.dot(rows.T, part.astype(jnp.float32), precision=lax.Precision.HIGHEST)
        partial = term if partial is None else partial + term

    block_rows = partial.shape[0] // tensors
    grad_part = lax.dynamic_slice_in_dim(partial, me_t * block_rows, block_rows, axis=0)
    for s in range(1, tensors):
        dest = (me_t + s) % tensors
        piece = lax.dynamic_slice_in_dim(partial, dest * block_rows, block_rows, axis=0)
        grad_part = grad_part + shifted(piece, "tensor", tensors, s)
    grad_part = grad_part / length.astype(jnp.float32)
    grad_flat = grad_part.reshape(1, -1).astype(jnp.bfloat16)

    grads = [grad_flat] + [shifted(grad_flat, "dp", dps, s) for s in range(1, dps)]
    grads = jnp.concatenate(grads, axis=0)
    scores = jnp.dot(grads, query_rows.T, preferred_element_type=jnp.float32)
    table = (
        query_decision[:, None] == jnp.arange(DECISIONS, dtype=jnp.int32)[None, :]
    ).astype(jnp.float32)
    partial_dec = jnp.dot(scores, table, precision=lax.Precision.HIGHEST)

    total = partial_dec[0:1]
    for s in range(1, dps):
        total = total + shifted(partial_dec[s : s + 1], "dp", dps, -s)

    peers = tensors * layers
    if peers <= 4:
        gathered = [shifted(total, ("tensor", "layer"), peers, s) for s in range(1, peers)]
        total = total + sum(gathered)
    else:
        total = lax.psum(total, ("tensor", "layer"))
    return total


def solution(mesh):
    in_specs = (
        P("layer", ("groups", "dp"), None, "tensor"),
        P("layer", ("groups", "dp"), "tensor", None),
        P("layer", "tensor", None),
        P("layer", None, None),
        P("layer", "dp", "tensor"),
        P(("groups", "dp")),
        P("dp"),
    )
    out_specs = P(("groups", "dp"), None)
    return jax.shard_map(body, mesh=mesh, in_specs=in_specs, out_specs=out_specs, check_vma=False)
```

```python
import jax
import jax.numpy as jnp
from jax import lax
from jax.sharding import PartitionSpec as P

DECISIONS = 1024


def shifted(x, axis, size, shift):
    return lax.ppermute(x, axis, [(i, (i + shift) % size) for i in range(size)])


def body_inner(hidden_in, out_grad, proj_in, proj_out, query_grads, lengths, query_decision):
    tensors = lax.axis_size("tensor")
    dps = lax.axis_size("dp")
    layers = lax.axis_size("layer")
    me_t = lax.axis_index("tensor")
    hidden_rows = hidden_in[0, 0]
    grad_rows = out_grad[0, 0]
    query_rows = query_grads[0]
    length = lengths[0]
    seq_shard = grad_rows.shape[0]

    positions = me_t * seq_shard + jnp.arange(seq_shard, dtype=jnp.int32)
    live = (positions < length).astype(jnp.float32)
    right = jnp.dot(grad_rows, proj_out[0], preferred_element_type=jnp.float32)
    right = (right * live[:, None]).astype(jnp.bfloat16)
    received = [right] + [shifted(right, "tensor", tensors, s) for s in range(1, tensors)]

    left = jnp.dot(hidden_rows, proj_in[0], preferred_element_type=jnp.float32)
    partial = None
    for s, part in enumerate(received):
        owner = (me_t - s) % tensors
        rows = lax.dynamic_slice_in_dim(left, owner * seq_shard, seq_shard, axis=0)
        term = jnp.dot(rows.T, part.astype(jnp.float32), precision=lax.Precision.HIGHEST)
        partial = term if partial is None else partial + term

    block_rows = partial.shape[0] // tensors
    grad_part = lax.dynamic_slice_in_dim(partial, me_t * block_rows, block_rows, axis=0)
    for s in range(1, tensors):
        dest = (me_t + s) % tensors
        piece = lax.dynamic_slice_in_dim(partial, dest * block_rows, block_rows, axis=0)
        grad_part = grad_part + shifted(piece, "tensor", tensors, s)
    grad_part = grad_part / length.astype(jnp.float32)
    grad_flat = grad_part.reshape(1, -1).astype(jnp.bfloat16)

    got = []
    for s in range(1, dps):
        got.append(shifted(grad_flat, "dp", dps, s))
    grads = jnp.concatenate([grad_flat] + got, axis=0)
    scores = jnp.dot(grads, query_rows.T, preferred_element_type=jnp.float32)
    table = (
        query_decision[:, None] == jnp.arange(DECISIONS, dtype=jnp.int32)[None, :]
    ).astype(jnp.float32)
    partial_dec = jnp.dot(scores, table, precision=lax.Precision.HIGHEST)

    total = partial_dec[0:1]
    for s in range(1, dps):
        total = total + shifted(partial_dec[s : s + 1], "dp", dps, -s)

    peers = tensors * layers
    if peers <= 4:
        gathered = [shifted(total, ("tensor", "layer"), peers, s) for s in range(1, peers)]
        total = total + sum(gathered)
    else:
        total = lax.psum(total, ("tensor", "layer"))
    return total


def solution(mesh):
    in_specs = (
        P("layer", ("groups", "dp"), None, "tensor"),
        P("layer", ("groups", "dp"), "tensor", None),
        P("layer", "tensor", None),
        P("layer", None, None),
        P("layer", "dp", "tensor"),
        P(("groups", "dp")),
        P("dp"),
    )
    out_specs = P(("groups", "dp"), None)
    return jax.shard_map(body_inner, mesh=mesh, in_specs=in_specs, out_specs=out_specs, check_vma=False)
```

```python
import jax
import jax.numpy as jnp
from jax import lax
from jax.sharding import PartitionSpec as P

DECISIONS = 1024


def shifted(x, axis, size, shift):
    return lax.ppermute(x, axis, [(i, (i + shift) % size) for i in range(size)])


def body_inner(hidden_in, out_grad, proj_in, proj_out, query_grads, lengths, query_decision):
    tensors = lax.axis_size("tensor")
    dps = lax.axis_size("dp")
    layers = lax.axis_size("layer")
    me_t = lax.axis_index("tensor")
    hidden_rows = hidden_in[0, 0]
    grad_rows = out_grad[0, 0]
    query_rows = query_grads[0]
    length = lengths[0]
    seq_shard = grad_rows.shape[0]

    positions = me_t * seq_shard + jnp.arange(seq_shard, dtype=jnp.int32)
    live = (positions < length).astype(jnp.float32)
    right = jnp.dot(grad_rows, proj_out[0], preferred_element_type=jnp.float32)
    right = (right * live[:, None]).astype(jnp.bfloat16)
    received = [right] + [shifted(right, "tensor", tensors, s) for s in range(1, tensors)]

    left = jnp.dot(hidden_rows, proj_in[0], preferred_element_type=jnp.float32)
    partial = None
    for s, part in enumerate(received):
        owner = (me_t - s) % tensors
        rows = lax.dynamic_slice_in_dim(left, owner * seq_shard, seq_shard, axis=0)
        term = jnp.dot(rows.T, part.astype(jnp.float32), precision=lax.Precision.HIGHEST)
        partial = term if partial is None else partial + term

    block_rows = partial.shape[0] // tensors
    grad_part = lax.dynamic_slice_in_dim(partial, me_t * block_rows, block_rows, axis=0)
    for s in range(1, tensors):
        dest = (me_t + s) % tensors
        piece = lax.dynamic_slice_in_dim(partial, dest * block_rows, block_rows, axis=0)
        grad_part = grad_part + shifted(piece, "tensor", tensors, s)
    grad_part = grad_part / length.astype(jnp.float32)
    grad_flat = grad_part.reshape(1, -1).astype(jnp.bfloat16)

    got = []
    for s in range(1, dps):
        got.append(shifted(grad_flat, "dp", dps, s))
    grads = jnp.concatenate([grad_flat] + got, axis=0)
    scores = jnp.dot(grads, query_rows.T, preferred_element_type=jnp.float32)
    table = (
        query_decision[:, None] == jnp.arange(DECISIONS, dtype=jnp.int32)[None, :]
    ).astype(jnp.float32)
    partial_dec = jnp.dot(scores, table, precision=lax.Precision.HIGHEST)

    total = partial_dec[0:1]
    for s in range(1, dps):
        total = total + shifted(partial_dec[s : s + 1], "dp", dps, -s)

    peers = tensors * layers
    if peers in (2, 4):
        flip = [
            lax.ppermute(total, ("tensor", "layer"), [(i, i ^ m) for i in range(peers)])
            for m in range(1, peers)
        ]
        total = total + flip[0]
        if peers == 4:
            total = total + (flip[1] + flip[2])
    elif peers > 1:
        total = lax.psum(total, ("tensor", "layer"))
    return total


def solution(mesh):
    in_specs = (
        P("layer", ("groups", "dp"), None, "tensor"),
        P("layer", ("groups", "dp"), "tensor", None),
        P("layer", "tensor", None),
        P("layer", None, None),
        P("layer", "dp", "tensor"),
        P(("groups", "dp")),
        P("dp"),
    )
    out_specs = P(("groups", "dp"), None)
    return jax.shard_map(body_inner, mesh=mesh, in_specs=in_specs, out_specs=out_specs, check_vma=False)
```
